128 devices in a mesh: dp: 128 (over y, z, x, core).
Axes of the slice: x: 4, y: 4, z: 4, core: 2. Of those that a mesh axis runs over, the one named last changes fastest.
Arguments:
- spikes: bfloat16 [512, 256, 256], P('dp'), may hold values from -6 to 6
- block_lists: int32 [512, 2], P('dp'), may hold values from 0 to 2047, as said below
- bin_counts: int32 [512], P('dp'), may hold values from 1 to 256, as said below
- readin_table: bfloat16 [2048, 128, 1024], P('dp'), may hold values from -0.375 to 0.375
- norm_gain: float32 [1024], replicated, may hold values from 0.1 to 1.9
- w_in: bfloat16 [1024, 2048], replicated, may hold values from -0.1875 to 0.1875
- w_out: bfloat16 [2048, 1024], replicated, may hold values from -0.125 to 0.125
- cotangent: bfloat16 [512, 256, 1024], P(None, 'dp'), may hold values from -6 to 6
Outputs:
- encoded: bfloat16 [512, 256, 1024], P(None, 'dp')
- readin_grad: bfloat16 [2048, 128, 1024], P('dp')
The draws below stay inside these ranges and needn't reach their ends.
Inputs may be any that keep to these rules, and one draw needn't show every extreme that they name: `block_lists`: block k is held by device k // 16. The sessions of device d are d * 4 to (d + 1) * 4 - 1; of their 8 entries exactly 1 name blocks held by each of the devices d, d + 1, ..., d + 7, counted modulo the number of devices. `bin_counts`: among the sessions of every device one has all 256 bins valid.
All inputs are finite; a program needn't handle non-finite values.
Results may differ from the reference program's by a relative error of at most 0.0056.
Values may be sent and summed in bfloat16 or wider, within the bound.
No kernel may reach another device: no remote copies, remote signals or barrier semaphores. Data moves between devices by JAX's collectives and lax.ppermute only.
A program may use at most 128 MiB of HBM per device.

```python
import jax
import jax.numpy as jnp
from jax import lax

D = 1024
FF = 2048
UB = 128
NB = 2
SESS_DEV = 4
TAB_DEV = 16
CAP = 1
SESSIONS = 512
BINS = 256
BLOCKS = 2048
N_DP = 128


def draw_block_lists(key, part):
    devices = SESSIONS // SESS_DEV
    slot_count = SESS_DEV * NB
    base_key = jax.random.fold_in(key, 11)
    first, second, third = jax.random.split(base_key, 3)
    pattern = jnp.arange(slot_count, dtype=jnp.int32) // CAP
    device_keys = jax.random.split(first, devices)
    offsets = jax.vmap(lambda one_key: jax.random.permutation(one_key, pattern))(device_keys)
    local_rows = jax.random.randint(second, (devices, slot_count), 0, TAB_DEV)
    chosen = jax.random.randint(third, (devices, 1), 0, slot_count)
    local_rows = jnp.where(jnp.arange(slot_count)[None, :] == chosen, TAB_DEV - 1, local_rows)
    owners = jnp.mod(jnp.arange(devices, dtype=jnp.int32)[:, None] + offsets, devices)
    return (owners * TAB_DEV + local_rows).reshape(SESSIONS, NB).astype(jnp.int32)


def draw_bin_counts(key, part):
    devices = SESSIONS // SESS_DEV
    base_key = jax.random.fold_in(key, 23)
    first, second = jax.random.split(base_key)
    counts = jax.random.randint(first, (devices, SESS_DEV), 1, BINS + 1)
    chosen = jax.random.randint(second, (devices, 1), 0, SESS_DEV)
    counts = jnp.where(jnp.arange(SESS_DEV)[None, :] == chosen, BINS, counts)
    return counts.reshape(SESSIONS).astype(jnp.int32)


def steps_of(own_key, shape, cuts, least, high):
    gain = 1.0
    for dim, blocks in cuts:
        steps = jax.random.uniform(jax.random.fold_in(jax.random.fold_in(own_key, 6), dim), (blocks,), jnp.float32, least / len(cuts), high / len(cuts))
        gain = gain * jnp.repeat(jnp.exp(steps), shape[dim] // blocks).reshape((-1,) + (1,) * (len(shape) - 1 - dim))
    return gain


def normal_values(key, extent, width, bound, shards=(), held_as=jnp.bfloat16):
    loudness = steps_of(key, extent, shards, -0.22, 0.18) if shards else 1.0
    array = jax.random.normal(key, extent, jnp.float32) * width * loudness
    return jnp.minimum(jnp.maximum(array, -bound), bound).astype(held_as)


def setup_inputs(seed: int = 0) -> dict:
    splits = jax.random.split(jax.random.key(seed), 9)
    spikes = normal_values(splits[0], (SESSIONS, BINS, NB * UB), 1.0, 6.0, ((0, 128),))
    block_lists = draw_block_lists(jax.random.fold_in(splits[8], 71), 0)
    bin_counts = draw_bin_counts(jax.random.fold_in(splits[8], 71), 0)
    readin_table = normal_values(splits[3], (BLOCKS, UB, D), (NB * UB) ** -0.5, 0.375, ((0, 128),))
    norm_gain = jnp.clip(1.0 + 0.18 * jax.random.normal(splits[4], (D,), jnp.float32), 0.1, 1.9)
    w_in = normal_values(splits[5], (D, FF), D ** -0.5, 0.1875)
    w_out = normal_values(splits[6], (FF, D), FF ** -0.5, 0.125)
    cotangent = normal_values(splits[7], (SESSIONS, BINS, D), 1.0, 6.0, ((1, 128),))
    return {"spikes": spikes, "block_lists": block_lists, "bin_counts": bin_counts, "readin_table": readin_table, "norm_gain": norm_gain, "w_in": w_in, "w_out": w_out, "cotangent": cotangent}


EPS = 1e-06

def gelu_tanh(values):
    return jax.nn.gelu(values, approximate=True)

def encode_rows(latent_rows, norm_gain, w_in, w_out, cot_rows):
    inputs = latent_rows.astype(jnp.float32)
    mean_square = lax.optimization_barrier(jnp.mean(inputs * inputs, axis=-1, keepdims=True))
    inverse_rms = lax.rsqrt(mean_square + EPS)
    normed = (inputs * inverse_rms * norm_gain).astype(jnp.bfloat16)
    hidden_pre = jnp.dot(normed, w_in, preferred_element_type=jnp.float32)
    activated, pullback = jax.vjp(gelu_tanh, hidden_pre)
    activated = activated.astype(jnp.bfloat16)
    encoded = (inputs + jnp.dot(activated, w_out, preferred_element_type=jnp.float32)).astype(jnp.bfloat16)
    grad_activated = lax.dot_general(cot_rows, w_out, (((1,), (1,)), ((), ())), preferred_element_type=jnp.float32)
    grad_hidden = pullback(grad_activated)[0].astype(jnp.bfloat16)
    grad_normed = lax.dot_general(grad_hidden, w_in, (((1,), (1,)), ((), ())), preferred_element_type=jnp.float32)
    scaled = grad_normed * norm_gain
    grad_inputs = inverse_rms * scaled - inputs * (inverse_rms * inverse_rms * inverse_rms) * lax.optimization_barrier(jnp.mean(scaled * inputs, axis=-1, keepdims=True))
    returned = (cot_rows.astype(jnp.float32) + grad_inputs).astype(jnp.bfloat16)
    return (encoded, returned)

def reference(spikes, block_lists, bin_counts, readin_table, norm_gain, w_in, w_out, cotangent):
    slot_count = SESS_DEV * NB
    spikes_dev = spikes.reshape(N_DP, SESS_DEV, BINS, NB, UB)
    lists_dev = block_lists.reshape(N_DP, slot_count).astype(jnp.int32)
    counts_dev = bin_counts.reshape(N_DP, SESS_DEV)
    cot_dev = cotangent.reshape(N_DP, SESS_DEV, BINS, D)

    def device_step(total, items):
        spikes_here, lists_here, counts_here, cot_here = items
        weights = jnp.take(readin_table, lists_here, axis=0).astype(jnp.float32).reshape(SESS_DEV, NB, UB, D)
        spikes_wide = spikes_here.astype(jnp.float32)
        latent = jnp.einsum('stnu,snud->std', spikes_wide, weights, precision=lax.Precision.HIGHEST)
        valid = (lax.broadcasted_iota(jnp.int32, (SESS_DEV, BINS), 1) < counts_here[:, None]).astype(jnp.float32)[:, :, None]
        latent = (latent * valid).astype(jnp.bfloat16)
        encoded, returned = encode_rows(latent.reshape(-1, D), norm_gain, w_in, w_out, cot_here.reshape(-1, D))
        grad_latent = (returned.reshape(SESS_DEV, BINS, D).astype(jnp.float32) * valid).astype(jnp.bfloat16)
        slot_grads = jnp.einsum('stnu,std->snud', spikes_wide, grad_latent.astype(jnp.float32), precision=lax.Precision.HIGHEST)
        total = total.at[lists_here].add(slot_grads.reshape(slot_count, UB, D))
        return (total, encoded.reshape(SESS_DEV, BINS, D))
    start = jnp.zeros((BLOCKS, UB, D), jnp.float32)
    total, encoded = lax.scan(device_step, start, (spikes_dev, lists_dev, counts_dev, cot_dev))
    return (encoded.reshape(SESSIONS, BINS, D), total.astype(jnp.bfloat16))
```

```python
import jax
import jax.numpy as jnp
from jax import lax
from jax.sharding import PartitionSpec as P

EPS = 1e-06


def from_behind(array, axis, by):
    count = lax.axis_size(axis)
    return lax.ppermute(array, axis, [(i, (i + by) % count) for i in range(count)])


def gelu_tanh(values):
    return jax.nn.gelu(values, approximate=True)


def encode_rows(latent_rows, norm_gain, w_in, w_out, cot_rows):
    inputs = latent_rows.astype(jnp.float32)
    mean_square = jnp.mean(inputs * inputs, axis=-1, keepdims=True)
    inverse_rms = lax.rsqrt(mean_square + EPS)
    normed = (inputs * inverse_rms * norm_gain).astype(jnp.bfloat16)
    hidden_pre = jnp.dot(normed, w_in, preferred_element_type=jnp.float32)
    activated, pullback = jax.vjp(gelu_tanh, hidden_pre)
    activated = activated.astype(jnp.bfloat16)
    encoded = (inputs + jnp.dot(activated, w_out, preferred_element_type=jnp.float32)).astype(
        jnp.bfloat16
    )
    grad_activated = lax.dot_general(
        cot_rows, w_out, (((1,), (1,)), ((), ())), preferred_element_type=jnp.float32
    )
    grad_hidden = pullback(grad_activated)[0].astype(jnp.bfloat16)
    grad_normed = lax.dot_general(
        grad_hidden, w_in, (((1,), (1,)), ((), ())), preferred_element_type=jnp.float32
    )
    scaled = grad_normed * norm_gain
    grad_inputs = inverse_rms * scaled - inputs * (
        inverse_rms * inverse_rms * inverse_rms
    ) * jnp.mean(scaled * inputs, axis=-1, keepdims=True)
    returned = (cot_rows.astype(jnp.float32) + grad_inputs).astype(jnp.bfloat16)
    return (encoded, returned)


def on_device(spikes, block_lists, bin_counts, readin_table, norm_gain, w_in, w_out, cotangent):
    devices = lax.axis_size("dp")
    me = lax.axis_index("dp")
    sessions_here, bins_all, unit_columns = spikes.shape
    table_rows, unit_block, latent_width = readin_table.shape
    blocks_per = unit_columns // unit_block
    slot_count = sessions_here * blocks_per
    near = slot_count

    flat_lists = block_lists.reshape(slot_count)
    offsets = jnp.mod(flat_lists // table_rows - me, devices)
    local_rows = jnp.mod(flat_lists, table_rows)
    slot_ids = jnp.arange(slot_count, dtype=jnp.int32)
    match = offsets[None, :] == jnp.arange(near, dtype=jnp.int32)[:, None]
    slot_of = jnp.sum(jnp.where(match, slot_ids[None, :], 0), axis=1)
    row_of = jnp.sum(jnp.where(match, local_rows[None, :], 0), axis=1)

    rows_held = [row_of[0:1]]
    for offset in range(1, near):
        rows_held.append(from_behind(row_of[offset : offset + 1], "dp", offset))
    fetched = [lax.dynamic_slice_in_dim(readin_table, row_of[0], 1, axis=0)]
    for offset in range(1, near):
        block = lax.dynamic_slice_in_dim(readin_table, rows_held[offset][0], 1, axis=0)
        fetched.append(from_behind(block, "dp", -offset))

    cot_here = lax.all_to_all(cotangent, "dp", split_axis=0, concat_axis=1, tiled=True)

    by_offset = jnp.concatenate(fetched, axis=0)
    by_slot = jnp.take(by_offset, offsets, axis=0)
    weights = by_slot.reshape(sessions_here, blocks_per * unit_block, latent_width)
    valid = (
        lax.broadcasted_iota(jnp.int32, (sessions_here, bins_all), 1) < bin_counts[:, None]
    ).astype(jnp.float32)[:, :, None]
    latent = jnp.einsum("stk,skd->std", spikes, weights, preferred_element_type=jnp.float32)
    latent = (latent * valid).astype(jnp.bfloat16)

    encoded, returned = encode_rows(
        latent.reshape(-1, latent_width),
        norm_gain,
        w_in,
        w_out,
        cot_here.reshape(-1, latent_width),
    )
    encoded_out = lax.all_to_all(
        encoded.reshape(sessions_here, bins_all, latent_width),
        "dp",
        split_axis=1,
        concat_axis=0,
        tiled=True,
    )

    grad_latent = (
        returned.reshape(sessions_here, bins_all, latent_width).astype(jnp.float32) * valid
    ).astype(jnp.bfloat16)
    spikes_split = spikes.reshape(sessions_here, bins_all, blocks_per, unit_block)
    slot_grads = jnp.einsum(
        "stnu,std->snud", spikes_split, grad_latent, preferred_element_type=jnp.float32
    ).astype(jnp.bfloat16)
    slot_grads = slot_grads.reshape(slot_count, unit_block, latent_width)

    pieces = [lax.dynamic_slice_in_dim(slot_grads, slot_of[0], 1, axis=0)]
    for offset in range(1, near):
        piece = lax.dynamic_slice_in_dim(slot_grads, slot_of[offset], 1, axis=0)
        pieces.append(from_behind(piece, "dp", offset))
    contributions = jnp.concatenate(pieces, axis=0)
    rows_in = jnp.concatenate(rows_held, axis=0)
    onehot = (rows_in[:, None] == jnp.arange(table_rows, dtype=jnp.int32)[None, :]).astype(
        jnp.bfloat16
    )
    total = jnp.einsum(
        "pr,pud->rud", onehot, contributions, preferred_element_type=jnp.float32
    )
    return (encoded_out, total.astype(jnp.bfloat16))


def solution(mesh):
    return jax.shard_map(
        on_device,
        mesh=mesh,
        in_specs=(
            P("dp", None, None),
            P("dp", None),
            P("dp"),
            P("dp", None, None),
            P(),
            P(),
            P(),
            P(None, "dp", None),
        ),
        out_specs=(P(None, "dp", None), P("dp", None, None)),
        check_vma=False,
    )
```

```python
import jax
import jax.numpy as jnp
from jax import lax
from jax.sharding import PartitionSpec as P

EPS = 1e-06


def from_behind(array, axis, by):
    count = lax.axis_size(axis)
    return lax.ppermute(array, axis, [(i, (i + by) % count) for i in range(count)])


def gelu_tanh(values):
    return jax.nn.gelu(values, approximate=True)


def encode_rows(latent_rows, norm_gain, w_in, w_out, cot_rows):
    inputs = latent_rows.astype(jnp.float32)
    mean_square = jnp.mean(inputs * inputs, axis=-1, keepdims=True)
    inverse_rms = lax.rsqrt(mean_square + EPS)
    normed = (inputs * inverse_rms * norm_gain).astype(jnp.bfloat16)
    hidden_pre = jnp.dot(normed, w_in, preferred_element_type=jnp.float32)
    activated, pullback = jax.vjp(gelu_tanh, hidden_pre)
    activated = activated.astype(jnp.bfloat16)
    encoded = (inputs + jnp.dot(activated, w_out, preferred_element_type=jnp.float32)).astype(
        jnp.bfloat16
    )
    grad_activated = lax.dot_general(
        cot_rows, w_out, (((1,), (1,)), ((), ())), preferred_element_type=jnp.float32
    )
    grad_hidden = pullback(grad_activated)[0].astype(jnp.bfloat16)
    grad_normed = lax.dot_general(
        grad_hidden, w_in, (((1,), (1,)), ((), ())), preferred_element_type=jnp.float32
    )
    scaled = grad_normed * norm_gain
    grad_inputs = inverse_rms * scaled - inputs * (
        inverse_rms * inverse_rms * inverse_rms
    ) * jnp.mean(scaled * inputs, axis=-1, keepdims=True)
    returned = (cot_rows.astype(jnp.float32) + grad_inputs).astype(jnp.bfloat16)
    return (encoded, returned)


def on_device(spikes, block_lists, bin_counts, readin_table, norm_gain, w_in, w_out, cotangent):
    devices = lax.axis_size("dp")
    me = lax.axis_index("dp")
    sessions_here, bins_all, unit_columns = spikes.shape
    table_rows, unit_block, latent_width = readin_table.shape
    blocks_per = unit_columns // unit_block
    slot_count = sessions_here * blocks_per
    near = slot_count

    flat_lists = block_lists.reshape(slot_count)
    offsets = jnp.mod(flat_lists // table_rows - me, devices)
    slot_ids = jnp.arange(slot_count, dtype=jnp.int32)
    match = offsets[None, :] == jnp.arange(near, dtype=jnp.int32)[:, None]
    slot_of = jnp.sum(jnp.where(match, slot_ids[None, :], 0), axis=1)

    all_lists = lax.all_gather(flat_lists, "dp", axis=0, tiled=False)
    sources = jnp.mod(me - jnp.arange(near, dtype=jnp.int32), devices)
    source_lists = jnp.take(all_lists, sources, axis=0)
    mine = (source_lists // table_rows) == me
    rows_in = jnp.sum(jnp.where(mine, jnp.mod(source_lists, table_rows), 0), axis=1)

    fetched = [lax.dynamic_slice_in_dim(readin_table, rows_in[0], 1, axis=0)]
    for offset in range(1, near):
        block = lax.dynamic_slice_in_dim(readin_table, rows_in[offset], 1, axis=0)
        fetched.append(from_behind(block, "dp", -offset))

    cot_here = lax.all_to_all(cotangent, "dp", split_axis=0, concat_axis=1, tiled=True)

    by_offset = jnp.concatenate(fetched, axis=0)
    by_slot = jnp.take(by_offset, offsets, axis=0)
    weights = by_slot.reshape(sessions_here, blocks_per * unit_block, latent_width)
    valid = (
        lax.broadcasted_iota(jnp.int32, (sessions_here, bins_all), 1) < bin_counts[:, None]
    ).astype(jnp.float32)[:, :, None]
    latent = jnp.einsum("stk,skd->std", spikes, weights, preferred_element_type=jnp.float32)
    latent = (latent * valid).astype(jnp.bfloat16)

    encoded, returned = encode_rows(
        latent.reshape(-1, latent_width),
        norm_gain,
        w_in,
        w_out,
        cot_here.reshape(-1, latent_width),
    )
    encoded_out = lax.all_to_all(
        encoded.reshape(sessions_here, bins_all, latent_width),
        "dp",
        split_axis=1,
        concat_axis=0,
        tiled=True,
    )

    grad_latent = (
        returned.reshape(sessions_here, bins_all, latent_width).astype(jnp.float32) * valid
    ).astype(jnp.bfloat16)
    slot_grads = jnp.einsum(
        "stk,std->skd", spikes, grad_latent, preferred_element_type=jnp.float32
    ).astype(jnp.bfloat16)
    slot_grads = slot_grads.reshape(slot_count, unit_block, latent_width)

    total = jnp.zeros((table_rows, unit_block, latent_width), jnp.float32)
    for offset in range(near):
        piece = lax.dynamic_slice_in_dim(slot_grads, slot_of[offset], 1, axis=0)
        if offset > 0:
            piece = from_behind(piece, "dp", offset)
        row = rows_in[offset]
        current = lax.dynamic_slice_in_dim(total, row, 1, axis=0)
        total = lax.dynamic_update_slice_in_dim(
            total, current + piece.astype(jnp.float32), row, axis=0
        )
    return (encoded_out, total.astype(jnp.bfloat16))


def solution(mesh):
    return jax.shard_map(
        on_device,
        mesh=mesh,
        in_specs=(
            P("dp", None, None),
            P("dp", None),
            P("dp"),
            P("dp", None, None),
            P(),
            P(),
            P(),
            P(None, "dp", None),
        ),
        out_specs=(P(None, "dp", None), P("dp", None, None)),
        check_vma=False,
    )
```

```python
import jax
import jax.numpy as jnp
from jax import lax
from jax.sharding import PartitionSpec as P

EPS = 1e-06


def from_behind(array, axis, by):
    count = lax.axis_size(axis)
    return lax.ppermute(array, axis, [(i, (i + by) % count) for i in range(count)])


def gelu_tanh(values):
    return jax.nn.gelu(values, approximate=True)


def encode_rows(latent_rows, norm_gain, w_in, w_out, cot_rows):
    inputs = latent_rows.astype(jnp.float32)
    mean_square = jnp.mean(inputs * inputs, axis=-1, keepdims=True)
    inverse_rms = lax.rsqrt(mean_square + EPS)
    normed = (inputs * inverse_rms * norm_gain).astype(jnp.bfloat16)
    hidden_pre = jnp.dot(normed, w_in, preferred_element_type=jnp.float32)
    activated, pullback = jax.vjp(gelu_tanh, hidden_pre)
    activated = activated.astype(jnp.bfloat16)
    encoded = (inputs + jnp.dot(activated, w_out, preferred_element_type=jnp.float32)).astype(
        jnp.bfloat16
    )
    grad_activated = lax.dot_general(
        cot_rows, w_out, (((1,), (1,)), ((), ())), preferred_element_type=jnp.float32
    )
    grad_hidden = lax.optimization_barrier(pullback(grad_activated)[0].astype(jnp.bfloat16))
    grad_normed = lax.dot_general(
        grad_hidden, w_in, (((1,), (1,)), ((), ())), preferred_element_type=jnp.float32
    )
    scaled = grad_normed * norm_gain
    grad_inputs = inverse_rms * scaled - inputs * (
        inverse_rms * inverse_rms * inverse_rms
    ) * jnp.mean(scaled * inputs, axis=-1, keepdims=True)
    returned = (cot_rows.astype(jnp.float32) + grad_inputs).astype(jnp.bfloat16)
    return (encoded, returned)


def on_device(spikes, block_lists, bin_counts, readin_table, norm_gain, w_in, w_out, cotangent):
    devices = lax.axis_size("dp")
    me = lax.axis_index("dp")
    sessions_here, bins_all, unit_columns = spikes.shape
    table_rows, unit_block, latent_width = readin_table.shape
    blocks_per = unit_columns // unit_block
    slot_count = sessions_here * blocks_per
    near = slot_count

    flat_lists = block_lists.reshape(slot_count)
    offsets = jnp.mod(flat_lists // table_rows - me, devices)
    slot_ids = jnp.arange(slot_count, dtype=jnp.int32)
    match = offsets[None, :] == jnp.arange(near, dtype=jnp.int32)[:, None]
    slot_of = jnp.sum(jnp.where(match, slot_ids[None, :], 0), axis=1)

    source_lists = flat_lists[None, :]
    span = 1
    while span < near:
        source_lists = jnp.concatenate(
            [source_lists, from_behind(source_lists, "dp", span)], axis=0
        )
        span *= 2
    source_lists = source_lists[:near]
    mine = (source_lists // table_rows) == me
    rows_in = jnp.sum(jnp.where(mine, jnp.mod(source_lists, table_rows), 0), axis=1)

    fetched = [lax.dynamic_slice_in_dim(readin_table, rows_in[0], 1, axis=0)]
    for offset in range(1, near):
        block = lax.dynamic_slice_in_dim(readin_table, rows_in[offset], 1, axis=0)
        fetched.append(from_behind(block, "dp", -offset))

    cot_here = lax.all_to_all(cotangent, "dp", split_axis=0, concat_axis=1, tiled=True)

    by_offset = jnp.concatenate(fetched, axis=0)
    by_slot = jnp.take(by_offset, offsets, axis=0)
    weights = by_slot.reshape(sessions_here, blocks_per * unit_block, latent_width)
    valid = (
        lax.broadcasted_iota(jnp.int32, (sessions_here, bins_all), 1) < bin_counts[:, None]
    ).astype(jnp.float32)[:, :, None]
    latent = jnp.einsum("stk,skd->std", spikes, weights, preferred_element_type=jnp.float32)
    latent = (latent * valid).astype(jnp.bfloat16)

    encoded, returned = encode_rows(
        latent.reshape(-1, latent_width),
        norm_gain,
        w_in,
        w_out,
        cot_here.reshape(-1, latent_width),
    )
    encoded_out = lax.all_to_all(
        encoded.reshape(sessions_here, bins_all, latent_width),
        "dp",
        split_axis=1,
        concat_axis=0,
        tiled=True,
    )

    grad_latent = (
        returned.reshape(sessions_here, bins_all, latent_width).astype(jnp.float32) * valid
    ).astype(jnp.bfloat16)
    slot_grads = jnp.einsum(
        "stk,std->skd", spikes, grad_latent, preferred_element_type=jnp.float32
    ).astype(jnp.bfloat16)
    slot_grads = slot_grads.reshape(slot_count, unit_block, latent_width)

    total = jnp.zeros((table_rows, unit_block, latent_width), jnp.float32)
    for offset in range(near):
        piece = lax.dynamic_slice_in_dim(slot_grads, slot_of[offset], 1, axis=0)
        if offset > 0:
            piece = from_behind(piece, "dp", offset)
        row = rows_in[offset]
        current = lax.dynamic_slice_in_dim(total, row, 1, axis=0)
        total = lax.dynamic_update_slice_in_dim(
            total, current + piece.astype(jnp.float32), row, axis=0
        )
    return (encoded_out, total.astype(jnp.bfloat16))


def solution(mesh):
    return jax.shard_map(
        on_device,
        mesh=mesh,
        in_specs=(
            P("dp", None, None),
            P("dp", None),
            P("dp"),
            P("dp", None, None),
            P(),
            P(),
            P(),
            P(None, "dp", None),
        ),
        out_specs=(P(None, "dp", None), P("dp", None, None)),
        check_vma=False,
    )
```

```python
import jax
import jax.numpy as jnp
from jax import lax
from jax.sharding import PartitionSpec as P

EPS = 1e-06


def from_behind(array, axis, by):
    count = lax.axis_size(axis)
    return lax.ppermute(array, axis, [(i, (i + by) % count) for i in range(count)])


def gelu_tanh(values):
    return jax.nn.gelu(values, approximate=True)


def encode_rows(latent_rows, norm_gain, w_in, w_out, cot_rows):
    inputs = latent_rows.astype(jnp.float32)
    mean_square = jnp.mean(inputs * inputs, axis=-1, keepdims=True)
    inverse_rms = lax.rsqrt(mean_square + EPS)
    normed = (inputs * inverse_rms * norm_gain).astype(jnp.bfloat16)
    hidden_pre = jnp.dot(normed, w_in, preferred_element_type=jnp.float32)
    activated, pullback = jax.vjp(gelu_tanh, hidden_pre)
    activated = activated.astype(jnp.bfloat16)
    encoded = (inputs + jnp.dot(activated, w_out, preferred_element_type=jnp.float32)).astype(
        jnp.bfloat16
    )
    grad_activated = lax.dot_general(
        cot_rows, w_out, (((1,), (1,)), ((), ())), preferred_element_type=jnp.float32
    )
    grad_hidden = lax.optimization_barrier(pullback(grad_activated)[0].astype(jnp.bfloat16))
    grad_normed = lax.dot_general(
        grad_hidden, w_in, (((1,), (1,)), ((), ())), preferred_element_type=jnp.float32
    )
    scaled = grad_normed * norm_gain
    grad_inputs = inverse_rms * scaled - inputs * (
        inverse_rms * inverse_rms * inverse_rms
    ) * jnp.mean(scaled * inputs, axis=-1, keepdims=True)
    returned = (cot_rows.astype(jnp.float32) + grad_inputs).astype(jnp.bfloat16)
    return (encoded, returned)


def on_device(spikes, block_lists, bin_counts, readin_table, norm_gain, w_in, w_out, cotangent):
    devices = lax.axis_size("dp")
    me = lax.axis_index("dp")
    sessions_here, bins_all, unit_columns = spikes.shape
    table_rows, unit_block, latent_width = readin_table.shape
    blocks_per = unit_columns // unit_block
    slot_count = sessions_here * blocks_per
    near = slot_count

    flat_lists = block_lists.reshape(slot_count)
    offsets = jnp.mod(flat_lists // table_rows - me, devices)
    slot_ids = jnp.arange(slot_count, dtype=jnp.int32)
    match = offsets[None, :] == jnp.arange(near, dtype=jnp.int32)[:, None]
    slot_of = jnp.sum(jnp.where(match, slot_ids[None, :], 0), axis=1)

    source_lists = flat_lists[None, :]
    span = 1
    while span < near:
        source_lists = jnp.concatenate(
            [source_lists, from_behind(source_lists, "dp", span)], axis=0
        )
        span *= 2
    source_lists = source_lists[:near]
    mine = (source_lists // table_rows) == me
    rows_in = jnp.sum(jnp.where(mine, jnp.mod(source_lists, table_rows), 0), axis=1)

    to_send = jnp.take(readin_table, rows_in, axis=0)
    fetched = [to_send[0:1]]
    for offset in range(1, near):
        fetched.append(from_behind(to_send[offset : offset + 1], "dp", -offset))

    cot_here = lax.all_to_all(cotangent, "dp", split_axis=0, concat_axis=1, tiled=True)

    by_offset = jnp.concatenate(fetched, axis=0)
    by_slot = jnp.take(by_offset, offsets, axis=0)
    weights = by_slot.reshape(sessions_here, blocks_per * unit_block, latent_width)
    valid = (
        lax.broadcasted_iota(jnp.int32, (bins_all, sessions_here), 0) < bin_counts[None, :]
    ).astype(jnp.float32)[:, :, None]
    latent = jnp.einsum("stk,skd->tsd", spikes, weights, preferred_element_type=jnp.float32)
    latent = (latent * valid).astype(jnp.bfloat16)

    encoded, returned = encode_rows(
        latent.reshape(-1, latent_width),
        norm_gain,
        w_in,
        w_out,
        jnp.transpose(cot_here, (1, 0, 2)).reshape(-1, latent_width),
    )
    encoded_out = lax.all_to_all(
        encoded.reshape(bins_all, sessions_here, latent_width),
        "dp",
        split_axis=0,
        concat_axis=1,
        tiled=True,
    )
    encoded_out = jnp.transpose(encoded_out, (1, 0, 2))

    grad_latent = (
        returned.reshape(bins_all, sessions_here, latent_width).astype(jnp.float32) * valid
    ).astype(jnp.bfloat16)
    slot_grads = jnp.einsum(
        "stk,tsd->skd", spikes, grad_latent, preferred_element_type=jnp.float32
    ).astype(jnp.bfloat16)
    slot_grads = slot_grads.reshape(slot_count, unit_block, latent_width)

    by_offset_grads = jnp.take(slot_grads, slot_of, axis=0)
    pieces = [by_offset_grads[0:1]]
    for offset in range(1, near):
        pieces.append(from_behind(by_offset_grads[offset : offset + 1], "dp", offset))
    contributions = jnp.concatenate(pieces, axis=0)
    onehot = (rows_in[:, None] == jnp.arange(table_rows, dtype=jnp.int32)[None, :]).astype(
        jnp.bfloat16
    )
    total = jnp.dot(
        onehot.T, contributions.reshape(near, -1), preferred_element_type=jnp.float32
    )
    total = total.astype(jnp.bfloat16).reshape(table_rows, unit_block, latent_width)
    return (encoded_out, total)


def solution(mesh):
    return jax.shard_map(
        on_device,
        mesh=mesh,
        in_specs=(
            P("dp", None, None),
            P("dp", None),
            P("dp"),
            P("dp", None, None),
            P(),
            P(),
            P(),
            P(None, "dp", None),
        ),
        out_specs=(P(None, "dp", None), P("dp", None, None)),
        check_vma=False,
    )
```

```python
import jax
import jax.numpy as jnp
from jax import lax
from jax.sharding import PartitionSpec as P

EPS = 1e-06


def from_behind(array, axis, by):
    count = lax.axis_size(axis)
    return lax.ppermute(array, axis, [(i, (i + by) % count) for i in range(count)])


def gelu_tanh(values):
    return jax.nn.gelu(values, approximate=True)


def encode_rows(latent_rows, norm_gain, w_in, w_out, cot_rows):
    inputs = latent_rows.astype(jnp.float32)
    mean_square = jnp.mean(inputs * inputs, axis=-1, keepdims=True)
    inverse_rms = lax.rsqrt(mean_square + EPS)
    normed = (inputs * inverse_rms * norm_gain).astype(jnp.bfloat16)
    hidden_pre = jnp.dot(normed, w_in, preferred_element_type=jnp.float32)
    activated, pullback = jax.vjp(gelu_tanh, hidden_pre)
    activated = activated.astype(jnp.bfloat16)
    encoded = (inputs + jnp.dot(activated, w_out, preferred_element_type=jnp.float32)).astype(
        jnp.bfloat16
    )
    grad_activated = lax.dot_general(
        cot_rows, w_out, (((1,), (1,)), ((), ())), preferred_element_type=jnp.float32
    )
    grad_hidden = lax.optimization_barrier(pullback(grad_activated)[0].astype(jnp.bfloat16))
    grad_normed = lax.dot_general(
        grad_hidden, w_in, (((1,), (1,)), ((), ())), preferred_element_type=jnp.float32
    )
    scaled = grad_normed * norm_gain
    grad_inputs = inverse_rms * scaled - inputs * (
        inverse_rms * inverse_rms * inverse_rms
    ) * jnp.mean(scaled * inputs, axis=-1, keepdims=True)
    returned = (cot_rows.astype(jnp.float32) + grad_inputs).astype(jnp.bfloat16)
    return (encoded, returned)


def on_device(spikes, block_lists, bin_counts, readin_table, norm_gain, w_in, w_out, cotangent):
    devices = lax.axis_size("dp")
    me = lax.axis_index("dp")
    sessions_here, bins_all, unit_columns = spikes.shape
    table_rows, unit_block, latent_width = readin_table.shape
    blocks_per = unit_columns // unit_block
    slot_count = sessions_here * blocks_per
    near = slot_count

    flat_lists = block_lists.reshape(slot_count)
    offsets = jnp.mod(flat_lists // table_rows - me, devices)
    slot_ids = jnp.arange(slot_count, dtype=jnp.int32)
    match = offsets[None, :] == jnp.arange(near, dtype=jnp.int32)[:, None]
    slot_of = jnp.sum(jnp.where(match, slot_ids[None, :], 0), axis=1)

    source_lists = flat_lists[None, :]
    span = 1
    while span < near:
        source_lists = jnp.concatenate(
            [source_lists, from_behind(source_lists, "dp", span)], axis=0
        )
        span *= 2
    source_lists = source_lists[:near]
    cotangent, source_lists = lax.optimization_barrier((cotangent, source_lists))
    mine = (source_lists // table_rows) == me
    rows_in = jnp.sum(jnp.where(mine, jnp.mod(source_lists, table_rows), 0), axis=1)

    to_send = jnp.take(readin_table, rows_in, axis=0)
    fetched = [to_send[0:1]]
    for offset in range(1, near):
        fetched.append(from_behind(to_send[offset : offset + 1], "dp", -offset))

    cot_here = lax.all_to_all(cotangent, "dp", split_axis=0, concat_axis=1, tiled=True)

    by_offset = jnp.concatenate(fetched, axis=0)
    by_slot = jnp.take(by_offset, offsets, axis=0)
    weights = by_slot.reshape(sessions_here, blocks_per * unit_block, latent_width)
    valid = (
        lax.broadcasted_iota(jnp.int32, (sessions_here, bins_all), 1) < bin_counts[:, None]
    ).astype(jnp.float32)[:, :, None]
    latent = jnp.einsum("stk,skd->std", spikes, weights, preferred_element_type=jnp.float32)
    latent = (latent * valid).astype(jnp.bfloat16)

    encoded, returned = encode_rows(
        latent.reshape(-1, latent_width),
        norm_gain,
        w_in,
        w_out,
        cot_here.reshape(-1, latent_width),
    )
    encoded_out = lax.all_to_all(
        encoded.reshape(sessions_here, bins_all, latent_width),
        "dp",
        split_axis=1,
        concat_axis=0,
        tiled=True,
    )

    grad_latent = (
        returned.reshape(sessions_here, bins_all, latent_width).astype(jnp.float32) * valid
    ).astype(jnp.bfloat16)
    slot_grads = jnp.einsum(
        "stk,std->skd", spikes, grad_latent, preferred_element_type=jnp.float32
    ).astype(jnp.bfloat16)
    slot_grads = slot_grads.reshape(slot_count, unit_block, latent_width)

    by_offset_grads = jnp.take(slot_grads, slot_of, axis=0)
    pieces = [by_offset_grads[0:1]]
    for offset in range(1, near):
        pieces.append(from_behind(by_offset_grads[offset : offset + 1], "dp", offset))
    contributions = jnp.concatenate(pieces, axis=0)
    onehot = (rows_in[:, None] == jnp.arange(table_rows, dtype=jnp.int32)[None, :]).astype(
        jnp.bfloat16
    )
    total = jnp.dot(
        onehot.T, contributions.reshape(near, -1), preferred_element_type=jnp.float32
    )
    total = total.astype(jnp.bfloat16).reshape(table_rows, unit_block, latent_width)
    return (encoded_out, total)


def solution(mesh):
    return jax.shard_map(
        on_device,
        mesh=mesh,
        in_specs=(
            P("dp", None, None),
            P("dp", None),
            P("dp"),
            P("dp", None, None),
            P(),
            P(),
            P(),
            P(None, "dp", None),
        ),
        out_specs=(P(None, "dp", None), P("dp", None, None)),
        check_vma=False,
    )
```

```python
import jax
import jax.numpy as jnp
from jax import lax
from jax.sharding import PartitionSpec as P

EPS = 1e-06


def from_behind(array, axis, by):
    count = lax.axis_size(axis)
    return lax.ppermute(array, axis, [(i, (i + by) % count) for i in range(count)])


def gelu_tanh(values):
    return jax.nn.gelu(values, approximate=True)


def encode_forward(latent_rows, norm_gain, w_in, w_out):
    inputs = latent_rows.astype(jnp.float32)
    mean_square = jnp.mean(inputs * inputs, axis=-1, keepdims=True)
    inverse_rms = lax.rsqrt(mean_square + EPS)
    normed = (inputs * inverse_rms * norm_gain).astype(jnp.bfloat16)
    hidden_pre = jnp.dot(normed, w_in, preferred_element_type=jnp.float32)
    activated = gelu_tanh(hidden_pre).astype(jnp.bfloat16)
    encoded = (inputs + jnp.dot(activated, w_out, preferred_element_type=jnp.float32)).astype(
        jnp.bfloat16
    )
    return encoded, (inputs, inverse_rms, hidden_pre)


def encode_backward(saved, norm_gain, w_in, w_out, cot_rows):
    inputs, inverse_rms, hidden_pre = saved
    grad_activated = lax.dot_general(
        cot_rows, w_out, (((1,), (1,)), ((), ())), preferred_element_type=jnp.float32
    )
    _, pullback = jax.vjp(gelu_tanh, hidden_pre)
    grad_hidden = lax.optimization_barrier(pullback(grad_activated)[0].astype(jnp.bfloat16))
    grad_normed = lax.dot_general(
        grad_hidden, w_in, (((1,), (1,)), ((), ())), preferred_element_type=jnp.float32
    )
    scaled = grad_normed * norm_gain
    grad_inputs = inverse_rms * scaled - inputs * (
        inverse_rms * inverse_rms * inverse_rms
    ) * jnp.mean(scaled * inputs, axis=-1, keepdims=True)
    returned = (cot_rows.astype(jnp.float32) + grad_inputs).astype(jnp.bfloat16)
    return returned


def on_device(spikes, block_lists, bin_counts, readin_table, norm_gain, w_in, w_out, cotangent):
    devices = lax.axis_size("dp")
    me = lax.axis_index("dp")
    sessions_here, bins_all, unit_columns = spikes.shape
    table_rows, unit_block, latent_width = readin_table.shape
    blocks_per = unit_columns // unit_block
    slot_count = sessions_here * blocks_per
    near = slot_count

    flat_lists = block_lists.reshape(slot_count)
    offsets = jnp.mod(flat_lists // table_rows - me, devices)
    slot_ids = jnp.arange(slot_count, dtype=jnp.int32)
    match = offsets[None, :] == jnp.arange(near, dtype=jnp.int32)[:, None]
    slot_of = jnp.sum(jnp.where(match, slot_ids[None, :], 0), axis=1)

    source_lists = flat_lists[None, :]
    span = 1
    while span < near:
        source_lists = jnp.concatenate(
            [source_lists, from_behind(source_lists, "dp", span)], axis=0
        )
        span *= 2
    source_lists = source_lists[:near]
    cotangent, source_lists = lax.optimization_barrier((cotangent, source_lists))
    mine = (source_lists // table_rows) == me
    rows_in = jnp.sum(jnp.where(mine, jnp.mod(source_lists, table_rows), 0), axis=1)

    to_send = jnp.take(readin_table, rows_in, axis=0)
    fetched = [to_send[0:1]]
    for offset in range(1, near):
        fetched.append(from_behind(to_send[offset : offset + 1], "dp", -offset))

    bins_here = cotangent.shape[1]
    cot_chunks = cotangent.reshape(devices, sessions_here, bins_here, latent_width)
    cot_chunks = lax.all_to_all(cot_chunks, "dp", split_axis=0, concat_axis=0, tiled=True)

    by_offset = jnp.concatenate(fetched, axis=0)
    by_slot = jnp.take(by_offset, offsets, axis=0)
    weights = by_slot.reshape(sessions_here, blocks_per * unit_block, latent_width)
    valid = (
        lax.broadcasted_iota(jnp.int32, (sessions_here, bins_all), 1) < bin_counts[:, None]
    ).astype(jnp.float32)[:, :, None]
    latent = jnp.einsum("stk,skd->std", spikes, weights, preferred_element_type=jnp.float32)
    latent = (latent * valid).astype(jnp.bfloat16)

    encoded, saved = encode_forward(latent.reshape(-1, latent_width), norm_gain, w_in, w_out)
    cot_chunks, encoded = lax.optimization_barrier((cot_chunks, encoded))
    cot_here = jnp.transpose(cot_chunks, (1, 0, 2, 3)).reshape(-1, latent_width)
    returned = encode_backward(saved, norm_gain, w_in, w_out, cot_here)
    encoded_chunks = jnp.transpose(
        encoded.reshape(sessions_here, devices, bins_here, latent_width), (1, 0, 2, 3)
    )
    encoded_chunks = lax.all_to_all(encoded_chunks, "dp", split_axis=0, concat_axis=0, tiled=True)
    encoded_out = encoded_chunks.reshape(devices * sessions_here, bins_here, latent_width)

    grad_latent = (
        returned.reshape(sessions_here, bins_all, latent_width).astype(jnp.float32) * valid
    ).astype(jnp.bfloat16)
    slot_grads = jnp.einsum(
        "stk,std->skd", spikes, grad_latent, preferred_element_type=jnp.float32
    ).astype(jnp.bfloat16)
    slot_grads = slot_grads.reshape(slot_count, unit_block, latent_width)

    by_offset_grads = jnp.take(slot_grads, slot_of, axis=0)
    pieces = [by_offset_grads[0:1]]
    for offset in range(1, near):
        pieces.append(from_behind(by_offset_grads[offset : offset + 1], "dp", offset))
    contributions = jnp.concatenate(pieces, axis=0)
    onehot = (rows_in[:, None] == jnp.arange(table_rows, dtype=jnp.int32)[None, :]).astype(
        jnp.bfloat16
    )
    total = jnp.dot(
        onehot.T, contributions.reshape(near, -1), preferred_element_type=jnp.float32
    )
    total = total.astype(jnp.bfloat16).reshape(table_rows, unit_block, latent_width)
    return (encoded_out, total)


def solution(mesh):
    return jax.shard_map(
        on_device,
        mesh=mesh,
        in_specs=(
            P("dp", None, None),
            P("dp", None),
            P("dp"),
            P("dp", None, None),
            P(),
            P(),
            P(),
            P(None, "dp", None),
        ),
        out_specs=(P(None, "dp", None), P("dp", None, None)),
        check_vma=False,
    )
```

```python
import jax
import jax.numpy as jnp
from jax import lax
from jax.sharding import PartitionSpec as P


EPS = 1e-06


def from_behind(array, axis, by):
    count = lax.axis_size(axis)
    return lax.ppermute(array, axis, [(i, (i + by) % count) for i in range(count)])


def gelu_tanh(values):
    return jax.nn.gelu(values, approximate=True)


def encode_forward(latent_rows, norm_gain, w_in, w_out):
    inputs = latent_rows.astype(jnp.float32)
    mean_square = jnp.mean(inputs * inputs, axis=-1, keepdims=True)
    inverse_rms = lax.rsqrt(mean_square + EPS)
    normed = (inputs * inverse_rms * norm_gain).astype(jnp.bfloat16)
    hidden_pre = jnp.dot(normed, w_in, preferred_element_type=jnp.float32)
    activated = gelu_tanh(hidden_pre).astype(jnp.bfloat16)
    encoded = (inputs + jnp.dot(activated, w_out, preferred_element_type=jnp.float32)).astype(
        jnp.bfloat16
    )
    return encoded, (inputs, inverse_rms, hidden_pre)


def encode_backward(saved, norm_gain, w_in, w_out, cot_rows):
    inputs, inverse_rms, hidden_pre = saved
    grad_activated = lax.dot_general(
        cot_rows, w_out, (((1,), (1,)), ((), ())), preferred_element_type=jnp.float32
    )
    _, pullback = jax.vjp(gelu_tanh, hidden_pre)
    grad_hidden = lax.optimization_barrier(pullback(grad_activated)[0].astype(jnp.bfloat16))
    grad_normed = lax.dot_general(
        grad_hidden, w_in, (((1,), (1,)), ((), ())), preferred_element_type=jnp.float32
    )
    scaled = grad_normed * norm_gain
    grad_inputs = inverse_rms * scaled - inputs * (
        inverse_rms * inverse_rms * inverse_rms
    ) * jnp.mean(scaled * inputs, axis=-1, keepdims=True)
    returned = (cot_rows.astype(jnp.float32) + grad_inputs).astype(jnp.bfloat16)
    return returned


def on_device(spikes, block_lists, bin_counts, readin_table, norm_gain, w_in, w_out, cotangent):
    devices = lax.axis_size("dp")
    me = lax.axis_index("dp")
    sessions_here, bins_all, unit_columns = spikes.shape
    table_rows, unit_block, latent_width = readin_table.shape
    blocks_per = unit_columns // unit_block
    slot_count = sessions_here * blocks_per
    near = slot_count

    flat_lists = block_lists.reshape(slot_count)
    offsets = jnp.mod(flat_lists // table_rows - me, devices)
    slot_ids = jnp.arange(slot_count, dtype=jnp.int32)
    match = offsets[None, :] == jnp.arange(near, dtype=jnp.int32)[:, None]
    slot_of = jnp.sum(jnp.where(match, slot_ids[None, :], 0), axis=1)

    source_lists = flat_lists[None, :]
    span = 1
    while span < near:
        source_lists = jnp.concatenate(
            [source_lists, from_behind(source_lists, "dp", span)], axis=0
        )
        span *= 2
    source_lists = source_lists[:near]
    cotangent, source_lists = lax.optimization_barrier((cotangent, source_lists))
    mine = (source_lists // table_rows) == me
    rows_in = jnp.sum(jnp.where(mine, jnp.mod(source_lists, table_rows), 0), axis=1)

    to_send = jnp.take(readin_table, rows_in, axis=0)
    fetched = [to_send[0:1]]
    for offset in range(1, near):
        fetched.append(from_behind(to_send[offset : offset + 1], "dp", -offset))

    bins_here = cotangent.shape[1]
    cot_chunks = cotangent.reshape(devices, sessions_here, bins_here, latent_width)
    cot_chunks = lax.all_to_all(cot_chunks, "dp", split_axis=0, concat_axis=0, tiled=True)

    by_offset = jnp.concatenate(fetched, axis=0)
    by_slot = jnp.take(by_offset, offsets, axis=0)
    weights = by_slot.reshape(sessions_here, blocks_per * unit_block, latent_width)
    valid = (
        lax.broadcasted_iota(jnp.int32, (sessions_here, bins_all), 1) < bin_counts[:, None]
    ).astype(jnp.float32)[:, :, None]
    latent = jnp.einsum("stk,skd->std", spikes, weights, preferred_element_type=jnp.float32)
    latent = (latent * valid).astype(jnp.bfloat16)

    encoded, saved = encode_forward(latent.reshape(-1, latent_width), norm_gain, w_in, w_out)
    cot_chunks, encoded = lax.optimization_barrier((cot_chunks, encoded))
    cot_here = jnp.transpose(cot_chunks, (1, 0, 2, 3)).reshape(-1, latent_width)
    returned = encode_backward(saved, norm_gain, w_in, w_out, cot_here)

    grad_latent = (
        returned.reshape(sessions_here, bins_all, latent_width).astype(jnp.float32) * valid
    ).astype(jnp.bfloat16)
    slot_grads = jnp.einsum(
        "stk,std->skd", spikes, grad_latent, preferred_element_type=jnp.float32
    ).astype(jnp.bfloat16)
    slot_grads = slot_grads.reshape(slot_count, unit_block, latent_width)

    by_offset_grads = jnp.take(slot_grads, slot_of, axis=0)
    pieces = [by_offset_grads[0:1]]
    for offset in range(1, near):
        pieces.append(from_behind(by_offset_grads[offset : offset + 1], "dp", offset))
    encoded_out = lax.all_to_all(
        encoded.reshape(sessions_here, bins_all, latent_width),
        "dp",
        split_axis=1,
        concat_axis=0,
        tiled=True,
    )
    contributions = jnp.concatenate(pieces, axis=0)
    onehot = (rows_in[:, None] == jnp.arange(table_rows, dtype=jnp.int32)[None, :]).astype(
        jnp.bfloat16
    )
    total = jnp.dot(
        onehot.T, contributions.reshape(near, -1), preferred_element_type=jnp.float32
    )
    total = total.astype(jnp.bfloat16).reshape(table_rows, unit_block, latent_width)
    return (encoded_out, total)


def solution(mesh):
    return jax.shard_map(
        on_device,
        mesh=mesh,
        in_specs=(
            P("dp", None, None),
            P("dp", None),
            P("dp"),
            P("dp", None, None),
            P(),
            P(),
            P(),
            P(None, "dp", None),
        ),
        out_specs=(P(None, "dp", None), P("dp", None, None)),
        check_vma=False,
    )
```

```python
import jax
import jax.numpy as jnp
from jax import lax
from jax.sharding import PartitionSpec as P

EPS = 1e-06


def from_behind(array, axis, by):
    count = lax.axis_size(axis)
    return lax.ppermute(array, axis, [(i, (i + by) % count) for i in range(count)])


def gelu_tanh(values):
    return jax.nn.gelu(values, approximate=True)


def encode_forward(latent_rows, norm_gain, w_in, w_out):
    inputs = latent_rows.astype(jnp.float32)
    mean_square = jnp.mean(inputs * inputs, axis=-1, keepdims=True)
    inverse_rms = lax.rsqrt(mean_square + EPS)
    normed = (inputs * inverse_rms * norm_gain).astype(jnp.bfloat16)
    hidden_pre = jnp.dot(normed, w_in, preferred_element_type=jnp.float32)
    activated = gelu_tanh(hidden_pre).astype(jnp.bfloat16)
    encoded = (inputs + jnp.dot(activated, w_out, preferred_element_type=jnp.float32)).astype(
        jnp.bfloat16
    )
    return encoded, (inputs, inverse_rms, hidden_pre)


def encode_backward(saved, norm_gain, w_in, w_out, cot_rows):
    inputs, inverse_rms, hidden_pre = saved
    grad_activated = lax.dot_general(
        cot_rows, w_out, (((1,), (1,)), ((), ())), preferred_element_type=jnp.float32
    )
    _, pullback = jax.vjp(gelu_tanh, hidden_pre)
    grad_hidden = lax.optimization_barrier(pullback(grad_activated)[0].astype(jnp.bfloat16))
    grad_normed = lax.dot_general(
        grad_hidden, w_in, (((1,), (1,)), ((), ())), preferred_element_type=jnp.float32
    )
    scaled = grad_normed * norm_gain
    grad_inputs = inverse_rms * scaled - inputs * (
        inverse_rms * inverse_rms * inverse_rms
    ) * jnp.mean(scaled * inputs, axis=-1, keepdims=True)
    returned = (cot_rows.astype(jnp.float32) + grad_inputs).astype(jnp.bfloat16)
    return returned


def on_device(spikes, block_lists, bin_counts, readin_table, norm_gain, w_in, w_out, cotangent):
    devices = lax.axis_size("dp")
    me = lax.axis_index("dp")
    sessions_here, bins_all, unit_columns = spikes.shape
    table_rows, unit_block, latent_width = readin_table.shape
    blocks_per = unit_columns // unit_block
    slot_count = sessions_here * blocks_per
    near = slot_count

    flat_lists = block_lists.reshape(slot_count)
    offsets = jnp.mod(flat_lists // table_rows - me, devices)
    slot_ids = jnp.arange(slot_count, dtype=jnp.int32)
    match = offsets[None, :] == jnp.arange(near, dtype=jnp.int32)[:, None]
    slot_of = jnp.sum(jnp.where(match, slot_ids[None, :], 0), axis=1)

    source_lists = flat_lists[None, :]
    span = 1
    while span < near:
        source_lists = jnp.concatenate(
            [source_lists, from_behind(source_lists, "dp", span)], axis=0
        )
        span *= 2
    source_lists = source_lists[:near]
    cotangent, source_lists = lax.optimization_barrier((cotangent, source_lists))
    mine = (source_lists // table_rows) == me
    rows_in = jnp.sum(jnp.where(mine, jnp.mod(source_lists, table_rows), 0), axis=1)

    to_send = jnp.take(readin_table, rows_in, axis=0)
    fetched = [to_send[0:1]]
    for offset in range(1, near):
        fetched.append(from_behind(to_send[offset : offset + 1], "dp", -offset))

    bins_here = cotangent.shape[1]
    chunk_rows = sessions_here * bins_here
    cot_chunks = cotangent.reshape(devices, chunk_rows, latent_width)
    cot_chunks = lax.all_to_all(cot_chunks, "dp", split_axis=0, concat_axis=0, tiled=True)

    by_offset = jnp.concatenate(fetched, axis=0)
    by_slot = jnp.take(by_offset, offsets, axis=0)
    weights = by_slot.reshape(sessions_here, blocks_per * unit_block, latent_width)
    rows_here = devices * chunk_rows
    bin_ids = (
        lax.broadcasted_iota(jnp.int32, (devices, sessions_here, bins_here), 0) * bins_here
        + lax.broadcasted_iota(jnp.int32, (devices, sessions_here, bins_here), 2)
    )
    valid = (bin_ids < bin_counts[None, :, None]).astype(jnp.float32).reshape(rows_here, 1)
    spikes_rows = jnp.transpose(
        spikes.reshape(sessions_here, devices, bins_here, unit_columns), (1, 0, 2, 3)
    ).reshape(rows_here, 1, unit_columns)
    row_session = lax.broadcasted_iota(jnp.int32, (devices, sessions_here, bins_here), 1)
    same = row_session.reshape(rows_here, 1, 1) == jnp.arange(sessions_here, dtype=jnp.int32)[
        None, :, None
    ]
    spread = jnp.where(same, spikes_rows, jnp.zeros((), spikes.dtype)).reshape(
        rows_here, sessions_here * unit_columns
    )
    latent = jnp.dot(
        spread, weights.reshape(sessions_here * unit_columns, latent_width),
        preferred_element_type=jnp.float32,
    )
    latent = (latent * valid).astype(jnp.bfloat16)

    encoded, saved = encode_forward(latent, norm_gain, w_in, w_out)
    cot_chunks, encoded = lax.optimization_barrier((cot_chunks, encoded))
    returned = encode_backward(saved, norm_gain, w_in, w_out, cot_chunks.reshape(-1, latent_width))
    encoded_chunks = lax.all_to_all(
        encoded.reshape(devices, chunk_rows, latent_width), "dp", split_axis=0, concat_axis=0, tiled=True
    )
    encoded_out = encoded_chunks.reshape(devices * sessions_here, bins_here, latent_width)

    grad_latent = (returned.astype(jnp.float32) * valid).astype(jnp.bfloat16)
    slot_grads = lax.dot_general(
        spread, grad_latent, (((0,), (0,)), ((), ())), preferred_element_type=jnp.float32
    ).astype(jnp.bfloat16)
    slot_grads = slot_grads.reshape(slot_count, unit_block, latent_width)

    by_offset_grads = jnp.take(slot_grads, slot_of, axis=0)
    pieces = [by_offset_grads[0:1]]
    for offset in range(1, near):
        pieces.append(from_behind(by_offset_grads[offset : offset + 1], "dp", offset))
    contributions = jnp.concatenate(pieces, axis=0)
    onehot = (rows_in[:, None] == jnp.arange(table_rows, dtype=jnp.int32)[None, :]).astype(
        jnp.bfloat16
    )
    total = jnp.dot(
        onehot.T, contributions.reshape(near, -1), preferred_element_type=jnp.float32
    )
    total = total.astype(jnp.bfloat16).reshape(table_rows, unit_block, latent_width)
    return (encoded_out, total)


def solution(mesh):
    return jax.shard_map(
        on_device,
        mesh=mesh,
        in_specs=(
            P("dp", None, None),
            P("dp", None),
            P("dp"),
            P("dp", None, None),
            P(),
            P(),
            P(),
            P(None, "dp", None),
        ),
        out_specs=(P(None, "dp", None), P("dp", None, None)),
        check_vma=False,
    )
```

```python
import jax
import jax.numpy as jnp
from jax import lax
from jax.sharding import PartitionSpec as P

EPS = 1e-06


def from_behind(array, axis, by):
    count = lax.axis_size(axis)
    return lax.ppermute(array, axis, [(i, (i + by) % count) for i in range(count)])


def gelu_tanh(values):
    return jax.nn.gelu(values, approximate=True)


def encode_forward(latent_rows, norm_gain, w_in, w_out):
    inputs = latent_rows.astype(jnp.float32)
    mean_square = jnp.mean(inputs * inputs, axis=-1, keepdims=True)
    inverse_rms = lax.rsqrt(mean_square + EPS)
    normed = (inputs * inverse_rms * norm_gain).astype(jnp.bfloat16)
    hidden_pre = jnp.dot(normed, w_in, preferred_element_type=jnp.float32)
    activated = gelu_tanh(hidden_pre).astype(jnp.bfloat16)
    encoded = (inputs + jnp.dot(activated, w_out, preferred_element_type=jnp.float32)).astype(
        jnp.bfloat16
    )
    return encoded, (inputs, inverse_rms, hidden_pre)


def encode_backward(saved, norm_gain, w_in, w_out, cot_rows):
    inputs, inverse_rms, hidden_pre = saved
    grad_activated = lax.dot_general(
        cot_rows, w_out, (((1,), (1,)), ((), ())), preferred_element_type=jnp.float32
    )
    _, pullback = jax.vjp(gelu_tanh, hidden_pre)
    grad_hidden = lax.optimization_barrier(pullback(grad_activated)[0].astype(jnp.bfloat16))
    grad_normed = lax.dot_general(
        grad_hidden, w_in, (((1,), (1,)), ((), ())), preferred_element_type=jnp.float32
    )
    scaled = grad_normed * norm_gain
    grad_inputs = inverse_rms * scaled - inputs * (
        inverse_rms * inverse_rms * inverse_rms
    ) * jnp.mean(scaled * inputs, axis=-1, keepdims=True)
    returned = (cot_rows.astype(jnp.float32) + grad_inputs).astype(jnp.bfloat16)
    return returned


def on_device(spikes, block_lists, bin_counts, readin_table, norm_gain, w_in, w_out, cotangent):
    devices = lax.axis_size("dp")
    me = lax.axis_index("dp")
    sessions_here, bins_all, unit_columns = spikes.shape
    table_rows, unit_block, latent_width = readin_table.shape
    blocks_per = unit_columns // unit_block
    slot_count = sessions_here * blocks_per
    near = slot_count

    flat_lists = block_lists.reshape(slot_count)
    offsets = jnp.mod(flat_lists // table_rows - me, devices)
    slot_ids = jnp.arange(slot_count, dtype=jnp.int32)
    match = offsets[None, :] == jnp.arange(near, dtype=jnp.int32)[:, None]
    slot_of = jnp.sum(jnp.where(match, slot_ids[None, :], 0), axis=1)

    half = near // 2
    first_round = [flat_lists[None, :]] + [
        from_behind(flat_lists[None, :], "dp", shift) for shift in range(1, half)
    ]
    first_round = jnp.concatenate(first_round, axis=0)
    source_lists = jnp.concatenate([first_round, from_behind(first_round, "dp", half)], axis=0)
    source_lists = source_lists[:near]
    cotangent, source_lists = lax.optimization_barrier((cotangent, source_lists))
    mine = (source_lists // table_rows) == me
    rows_in = jnp.sum(jnp.where(mine, jnp.mod(source_lists, table_rows), 0), axis=1)

    to_send = jnp.take(readin_table, rows_in, axis=0)
    fetched = [to_send[0:1]]
    for offset in range(1, near):
        fetched.append(from_behind(to_send[offset : offset + 1], "dp", -offset))

    bins_here = cotangent.shape[1]
    cot_chunks = cotangent.reshape(devices, sessions_here, bins_here, latent_width)
    cot_chunks = lax.all_to_all(cot_chunks, "dp", split_axis=0, concat_axis=0, tiled=True)

    by_offset = jnp.concatenate(fetched, axis=0)
    by_slot = jnp.take(by_offset, offsets, axis=0)
    weights = by_slot.reshape(sessions_here, blocks_per * unit_block, latent_width)
    valid = (
        lax.broadcasted_iota(jnp.int32, (sessions_here, bins_all), 1) < bin_counts[:, None]
    ).astype(jnp.float32)[:, :, None]
    latent = jnp.einsum("stk,skd->std", spikes, weights, preferred_element_type=jnp.float32)
    latent = (latent * valid).astype(jnp.bfloat16)

    encoded, saved = encode_forward(latent.reshape(-1, latent_width), norm_gain, w_in, w_out)
    cot_chunks, encoded = lax.optimization_barrier((cot_chunks, encoded))
    cot_here = jnp.transpose(cot_chunks, (1, 0, 2, 3)).reshape(-1, latent_width)
    returned = encode_backward(saved, norm_gain, w_in, w_out, cot_here)
    encoded_out = lax.all_to_all(
        encoded.reshape(sessions_here, bins_all, latent_width),
        "dp",
        split_axis=1,
        concat_axis=0,
        tiled=True,
    )

    grad_latent = (
        returned.reshape(sessions_here, bins_all, latent_width).astype(jnp.float32) * valid
    ).astype(jnp.bfloat16)
    slot_grads = jnp.einsum(
        "stk,std->skd", spikes, grad_latent, preferred_element_type=jnp.float32
    ).astype(jnp.bfloat16)
    slot_grads = slot_grads.reshape(slot_count, unit_block, latent_width)

    by_offset_grads = jnp.take(slot_grads, slot_of, axis=0)
    pieces = [by_offset_grads[0:1]]
    for offset in range(1, near):
        pieces.append(from_behind(by_offset_grads[offset : offset + 1], "dp", offset))
    contributions = jnp.concatenate(pieces, axis=0)
    onehot = (rows_in[:, None] == jnp.arange(table_rows, dtype=jnp.int32)[None, :]).astype(
        jnp.bfloat16
    )
    total = jnp.dot(
        onehot.T, contributions.reshape(near, -1), preferred_element_type=jnp.float32
    )
    total = total.astype(jnp.bfloat16).reshape(table_rows, unit_block, latent_width)
    return (encoded_out, total)


def solution(mesh):
    return jax.shard_map(
        on_device,
        mesh=mesh,
        in_specs=(
            P("dp", None, None),
            P("dp", None),
            P("dp"),
            P("dp", None, None),
            P(),
            P(),
            P(),
            P(None, "dp", None),
        ),
        out_specs=(P(None, "dp", None), P("dp", None, None)),
        check_vma=False,
    )
```

```python
import jax
import jax.numpy as jnp
from jax import lax
from jax.sharding import PartitionSpec as P

EPS = 1e-06


def from_behind(array, axis, by):
    count = lax.axis_size(axis)
    return lax.ppermute(array, axis, [(i, (i + by) % count) for i in range(count)])


def gelu_tanh(values):
    return jax.nn.gelu(values, approximate=True)


def encode_forward(latent_rows, norm_gain, w_in, w_out):
    inputs = latent_rows.astype(jnp.float32)
    mean_square = jnp.mean(inputs * inputs, axis=-1, keepdims=True)
    inverse_rms = lax.rsqrt(mean_square + EPS)
    normed = (inputs * inverse_rms * norm_gain).astype(jnp.bfloat16)
    hidden_pre = jnp.dot(normed, w_in, preferred_element_type=jnp.float32)
    activated = gelu_tanh(hidden_pre).astype(jnp.bfloat16)
    encoded = (inputs + jnp.dot(activated, w_out, preferred_element_type=jnp.float32)).astype(
        jnp.bfloat16
    )
    return encoded, (inputs, inverse_rms, hidden_pre)


def encode_backward(saved, norm_gain, w_in, w_out, cot_rows):
    inputs, inverse_rms, hidden_pre = saved
    grad_activated = lax.dot_general(
        cot_rows, w_out, (((1,), (1,)), ((), ())), preferred_element_type=jnp.float32
    )
    _, pullback = jax.vjp(gelu_tanh, hidden_pre)
    grad_hidden = lax.optimization_barrier(pullback(grad_activated)[0].astype(jnp.bfloat16))
    grad_normed = lax.dot_general(
        grad_hidden, w_in, (((1,), (1,)), ((), ())), preferred_element_type=jnp.float32
    )
    scaled = grad_normed * norm_gain
    grad_inputs = inverse_rms * scaled - inputs * (
        inverse_rms * inverse_rms * inverse_rms
    ) * jnp.mean(scaled * inputs, axis=-1, keepdims=True)
    returned = (cot_rows.astype(jnp.float32) + grad_inputs).astype(jnp.bfloat16)
    return returned


def on_device(spikes, block_lists, bin_counts, readin_table, norm_gain, w_in, w_out, cotangent):
    devices = lax.axis_size("dp")
    me = lax.axis_index("dp")
    sessions_here, bins_all, unit_columns = spikes.shape
    table_rows, unit_block, latent_width = readin_table.shape
    blocks_per = unit_columns // unit_block
    slot_count = sessions_here * blocks_per
    near = slot_count

    flat_lists = block_lists.reshape(slot_count)
    offsets = jnp.mod(flat_lists // table_rows - me, devices)
    slot_ids = jnp.arange(slot_count, dtype=jnp.int32)
    match = offsets[None, :] == jnp.arange(near, dtype=jnp.int32)[:, None]
    slot_of = jnp.sum(jnp.where(match, slot_ids[None, :], 0), axis=1)

    half = near // 2
    first_round = [flat_lists[None, :]] + [
        from_behind(flat_lists[None, :], "dp", shift) for shift in range(1, half)
    ]
    first_round = jnp.concatenate(first_round, axis=0)
    source_lists = jnp.concatenate([first_round, from_behind(first_round, "dp", half)], axis=0)
    source_lists = source_lists[:near]
    cotangent, source_lists = lax.optimization_barrier((cotangent, source_lists))
    mine = (source_lists // table_rows) == me
    rows_in = jnp.sum(jnp.where(mine, jnp.mod(source_lists, table_rows), 0), axis=1)

    to_send = jnp.take(readin_table, rows_in, axis=0)
    fetched = [to_send[0:1]]
    for offset in range(1, near):
        fetched.append(from_behind(to_send[offset : offset + 1], "dp", -offset))

    bins_here = cotangent.shape[1]
    cot_chunks = cotangent.reshape(devices, sessions_here, bins_here, latent_width)
    cot_chunks = lax.all_to_all(cot_chunks, "dp", split_axis=0, concat_axis=0, tiled=True)

    by_offset = jnp.concatenate(fetched, axis=0)
    by_slot = jnp.take(by_offset, offsets, axis=0)
    weights = by_slot.reshape(sessions_here, blocks_per * unit_block, latent_width)
    valid = (
        lax.broadcasted_iota(jnp.int32, (sessions_here, bins_all), 1) < bin_counts[:, None]
    ).astype(jnp.float32)[:, :, None]
    latent = jnp.einsum("stk,skd->std", spikes, weights, preferred_element_type=jnp.float32)
    latent = (latent * valid).astype(jnp.bfloat16)

    encoded, saved = encode_forward(latent.reshape(-1, latent_width), norm_gain, w_in, w_out)
    cot_chunks, encoded = lax.optimization_barrier((cot_chunks, encoded))
    cot_here = jnp.transpose(cot_chunks, (1, 0, 2, 3)).reshape(-1, latent_width)
    returned = encode_backward(saved, norm_gain, w_in, w_out, cot_here)
    encoded_out = lax.all_to_all(
        encoded.reshape(sessions_here, bins_all, latent_width),
        "dp",
        split_axis=1,
        concat_axis=0,
        tiled=True,
    )

    grad_latent = (
        returned.reshape(sessions_here, bins_all, latent_width).astype(jnp.float32) * valid
    ).astype(jnp.bfloat16)
    slot_grads = jnp.einsum(
        "stk,std->skd", spikes, grad_latent, preferred_element_type=jnp.float32
    ).astype(jnp.bfloat16)
    slot_grads = slot_grads.reshape(slot_count, unit_block, latent_width)

    by_offset_grads = jnp.take(slot_grads, slot_of, axis=0)
    pieces = [by_offset_grads[0:1]]
    for offset in range(1, near):
        pieces.append(from_behind(by_offset_grads[offset : offset + 1], "dp", offset))
    middle = near // 2
    encoded_out, pieces[middle] = lax.optimization_barrier((encoded_out, pieces[middle]))
    contributions = jnp.concatenate(pieces, axis=0)
    onehot = (rows_in[:, None] == jnp.arange(table_rows, dtype=jnp.int32)[None, :]).astype(
        jnp.bfloat16
    )
    total = jnp.dot(
        onehot.T, contributions.reshape(near, -1), preferred_element_type=jnp.float32
    )
    total = total.astype(jnp.bfloat16).reshape(table_rows, unit_block, latent_width)
    return (encoded_out, total)


def solution(mesh):
    return jax.shard_map(
        on_device,
        mesh=mesh,
        in_specs=(
            P("dp", None, None),
            P("dp", None),
            P("dp"),
            P("dp", None, None),
            P(),
            P(),
            P(),
            P(None, "dp", None),
        ),
        out_specs=(P(None, "dp", None), P("dp", None, None)),
        check_vma=False,
    )
```

```python
import jax
import jax.numpy as jnp
from jax import lax
from jax.sharding import PartitionSpec as P

EPS = 1e-06


def from_behind(array, axis, by):
    count = lax.axis_size(axis)
    return lax.ppermute(array, axis, [(i, (i + by) % count) for i in range(count)])


def gelu_tanh(values):
    return jax.nn.gelu(values, approximate=True)


def encode_forward(latent_rows, norm_gain, w_in, w_out):
    inputs = latent_rows.astype(jnp.float32)
    mean_square = jnp.mean(inputs * inputs, axis=-1, keepdims=True)
    inverse_rms = lax.rsqrt(mean_square + EPS)
    normed = (inputs * inverse_rms * norm_gain).astype(jnp.bfloat16)
    hidden_pre = jnp.dot(normed, w_in, preferred_element_type=jnp.float32)
    activated = gelu_tanh(hidden_pre).astype(jnp.bfloat16)
    encoded = (inputs + jnp.dot(activated, w_out, preferred_element_type=jnp.float32)).astype(
        jnp.bfloat16
    )
    return encoded, (inputs, inverse_rms, hidden_pre)


def encode_backward(saved, norm_gain, w_in, w_out, cot_rows):
    inputs, inverse_rms, hidden_pre = saved
    grad_activated = lax.dot_general(
        cot_rows, w_out, (((1,), (1,)), ((), ())), preferred_element_type=jnp.float32
    )
    _, pullback = jax.vjp(gelu_tanh, hidden_pre)
    grad_hidden = lax.optimization_barrier(pullback(grad_activated)[0].astype(jnp.bfloat16))
    grad_normed = lax.dot_general(
        grad_hidden, w_in, (((1,), (1,)), ((), ())), preferred_element_type=jnp.float32
    )
    scaled = grad_normed * norm_gain
    grad_inputs = inverse_rms * scaled - inputs * (
        inverse_rms * inverse_rms * inverse_rms
    ) * jnp.mean(scaled * inputs, axis=-1, keepdims=True)
    returned = (cot_rows.astype(jnp.float32) + grad_inputs).astype(jnp.bfloat16)
    return returned


def on_device(spikes, block_lists, bin_counts, readin_table, norm_gain, w_in, w_out, cotangent):
    devices = lax.axis_size("dp")
    me = lax.axis_index("dp")
    sessions_here, bins_all, unit_columns = spikes.shape
    table_rows, unit_block, latent_width = readin_table.shape
    blocks_per = unit_columns // unit_block
    slot_count = sessions_here * blocks_per
    near = slot_count

    flat_lists = block_lists.reshape(slot_count)
    offsets = jnp.mod(flat_lists // table_rows - me, devices)
    slot_ids = jnp.arange(slot_count, dtype=jnp.int32)
    match = offsets[None, :] == jnp.arange(near, dtype=jnp.int32)[:, None]
    slot_of = jnp.sum(jnp.where(match, slot_ids[None, :], 0), axis=1)

    half = near // 2
    first_round = [flat_lists[None, :]] + [
        from_behind(flat_lists[None, :], "dp", shift) for shift in range(1, half)
    ]
    first_round = jnp.concatenate(first_round, axis=0)
    source_lists = jnp.concatenate([first_round, from_behind(first_round, "dp", half)], axis=0)
    source_lists = source_lists[:near]
    cotangent, source_lists = lax.optimization_barrier((cotangent, source_lists))
    mine = (source_lists // table_rows) == me
    rows_in = jnp.sum(jnp.where(mine, jnp.mod(source_lists, table_rows), 0), axis=1)

    to_send = jnp.take(readin_table, rows_in, axis=0)
    fetched = [to_send[0:1]]
    for offset in range(1, near):
        fetched.append(from_behind(to_send[offset : offset + 1], "dp", -offset))

    bins_here = cotangent.shape[1]
    cot_chunks = cotangent.reshape(devices, sessions_here, bins_here, latent_width)
    cot_chunks = lax.all_to_all(cot_chunks, "dp", split_axis=0, concat_axis=0, tiled=True)

    by_offset = jnp.concatenate(fetched, axis=0)
    by_slot = jnp.take(by_offset, offsets, axis=0)
    weights = by_slot.reshape(sessions_here, blocks_per * unit_block, latent_width)
    valid = (
        lax.broadcasted_iota(jnp.int32, (sessions_here, bins_all), 1) < bin_counts[:, None]
    ).astype(jnp.float32)[:, :, None]
    latent = jnp.einsum("stk,skd->std", spikes, weights, preferred_element_type=jnp.float32)
    latent = (latent * valid).astype(jnp.bfloat16)

    encoded, saved = encode_forward(latent.reshape(-1, latent_width), norm_gain, w_in, w_out)
    cot_chunks, encoded = lax.optimization_barrier((cot_chunks, encoded))
    cot_here = jnp.transpose(cot_chunks, (1, 0, 2, 3)).reshape(-1, latent_width)
    returned = encode_backward(saved, norm_gain, w_in, w_out, cot_here)
    encoded_out = lax.all_to_all(
        encoded.reshape(sessions_here, bins_all, latent_width),
        "dp",
        split_axis=1,
        concat_axis=0,
        tiled=True,
    )

    grad_latent = (
        returned.reshape(sessions_here, bins_all, latent_width).astype(jnp.float32) * valid
    ).astype(jnp.bfloat16)
    slot_grads = jnp.einsum(
        "stk,std->skd", spikes, grad_latent, preferred_element_type=jnp.float32
    ).astype(jnp.bfloat16)
    slot_grads = slot_grads.reshape(slot_count, unit_block, latent_width)

    by_offset_grads = jnp.take(slot_grads, slot_of, axis=0)
    pieces = [by_offset_grads[0:1]]
    for offset in range(1, near):
        pieces.append(from_behind(by_offset_grads[offset : offset + 1], "dp", offset))
    middle = near // 2
    encoded_out, pieces[middle] = lax.optimization_barrier((encoded_out, pieces[middle]))
    contributions = jnp.concatenate(pieces, axis=0)
    hits = rows_in[None, :] == jnp.arange(table_rows, dtype=jnp.int32)[:, None]
    same_unit = (
        lax.broadcasted_iota(jnp.int32, (unit_block, unit_block), 0)
        == lax.broadcasted_iota(jnp.int32, (unit_block, unit_block), 1)
    )
    select_rows = (hits[:, None, :, None] & same_unit[None, :, None, :]).astype(jnp.bfloat16)
    select_rows = select_rows.reshape(table_rows * unit_block, near * unit_block)
    total = jnp.dot(
        select_rows,
        contributions.reshape(near * unit_block, latent_width),
        preferred_element_type=jnp.float32,
    )
    total = total.astype(jnp.bfloat16).reshape(table_rows, unit_block, latent_width)
    return (encoded_out, total)


def solution(mesh):
    return jax.shard_map(
        on_device,
        mesh=mesh,
        in_specs=(
            P("dp", None, None),
            P("dp", None),
            P("dp"),
            P("dp", None, None),
            P(),
            P(),
            P(),
            P(None, "dp", None),
        ),
        out_specs=(P(None, "dp", None), P("dp", None, None)),
        check_vma=False,
    )
```

```python
import jax
import jax.numpy as jnp
from jax import lax
from jax.sharding import PartitionSpec as P

EPS = 1e-06


def from_behind(array, axis, by):
    count = lax.axis_size(axis)
    return lax.ppermute(array, axis, [(i, (i + by) % count) for i in range(count)])


def gelu_tanh(values):
    return jax.nn.gelu(values, approximate=True)


def encode_forward(latent_rows, norm_gain, w_in, w_out):
    inputs = latent_rows.astype(jnp.float32)
    mean_square = jnp.mean(inputs * inputs, axis=-1, keepdims=True)
    inverse_rms = lax.rsqrt(mean_square + EPS)
    normed = (inputs * inverse_rms * norm_gain).astype(jnp.bfloat16)
    hidden_pre = jnp.dot(normed, w_in, preferred_element_type=jnp.float32)
    activated = gelu_tanh(hidden_pre).astype(jnp.bfloat16)
    encoded = (inputs + jnp.dot(activated, w_out, preferred_element_type=jnp.float32)).astype(
        jnp.bfloat16
    )
    return encoded, (inputs, inverse_rms, hidden_pre)


def encode_backward(saved, norm_gain, w_in, w_out, cot_rows):
    inputs, inverse_rms, hidden_pre = saved
    grad_activated = lax.dot_general(
        cot_rows, w_out, (((1,), (1,)), ((), ())), preferred_element_type=jnp.float32
    )
    _, pullback = jax.vjp(gelu_tanh, hidden_pre)
    grad_hidden = lax.optimization_barrier(pullback(grad_activated)[0].astype(jnp.bfloat16))
    grad_normed = lax.dot_general(
        grad_hidden, w_in, (((1,), (1,)), ((), ())), preferred_element_type=jnp.float32
    )
    scaled = grad_normed * norm_gain
    grad_inputs = inverse_rms * scaled - inputs * (
        inverse_rms * inverse_rms * inverse_rms
    ) * jnp.mean(scaled * inputs, axis=-1, keepdims=True)
    returned = (cot_rows.astype(jnp.float32) + grad_inputs).astype(jnp.bfloat16)
    return returned


def on_device(spikes, block_lists, bin_counts, readin_table, norm_gain, w_in, w_out, cotangent):
    devices = lax.axis_size("dp")
    me = lax.axis_index("dp")
    sessions_here, bins_all, unit_columns = spikes.shape
    table_rows, unit_block, latent_width = readin_table.shape
    blocks_per = unit_columns // unit_block
    slot_count = sessions_here * blocks_per
    near = slot_count

    flat_lists = block_lists.reshape(slot_count)
    offsets = jnp.mod(flat_lists // table_rows - me, devices)
    slot_ids = jnp.arange(slot_count, dtype=jnp.int32)
    match = offsets[None, :] == jnp.arange(near, dtype=jnp.int32)[:, None]
    slot_of = jnp.sum(jnp.where(match, slot_ids[None, :], 0), axis=1)

    half = near // 2
    first_round = [flat_lists[None, :]] + [
        from_behind(flat_lists[None, :], "dp", shift) for shift in range(1, half)
    ]
    first_round = jnp.concatenate(first_round, axis=0)
    source_lists = jnp.concatenate([first_round, from_behind(first_round, "dp", half)], axis=0)
    source_lists = source_lists[:near]
    cotangent, source_lists = lax.optimization_barrier((cotangent, source_lists))
    mine = (source_lists // table_rows) == me
    rows_in = jnp.sum(jnp.where(mine, jnp.mod(source_lists, table_rows), 0), axis=1)

    to_send = jnp.take(readin_table, rows_in, axis=0, mode="clip")
    fetched = [to_send[0:1]]
    for offset in range(1, near):
        fetched.append(from_behind(to_send[offset : offset + 1], "dp", -offset))

    bins_here = cotangent.shape[1]
    cot_chunks = cotangent.reshape(devices, sessions_here, bins_here, latent_width)
    cot_chunks = lax.all_to_all(cot_chunks, "dp", split_axis=0, concat_axis=0, tiled=True)

    by_offset = jnp.concatenate(fetched, axis=0)
    by_slot = jnp.take(by_offset, offsets, axis=0, mode="clip")
    weights = by_slot.reshape(sessions_here, blocks_per * unit_block, latent_width)
    valid = (
        lax.broadcasted_iota(jnp.int32, (sessions_here, bins_all), 1) < bin_counts[:, None]
    ).astype(jnp.float32)[:, :, None]
    latent = jnp.einsum("stk,skd->std", spikes, weights, preferred_element_type=jnp.float32)
    latent = (latent * valid).astype(jnp.bfloat16)

    encoded, saved = encode_forward(latent.reshape(-1, latent_width), norm_gain, w_in, w_out)
    cot_chunks, encoded = lax.optimization_barrier((cot_chunks, encoded))
    cot_here = jnp.transpose(cot_chunks, (1, 0, 2, 3)).reshape(-1, latent_width)
    returned = encode_backward(saved, norm_gain, w_in, w_out, cot_here)
    encoded_out = lax.all_to_all(
        encoded.reshape(sessions_here, bins_all, latent_width),
        "dp",
        split_axis=1,
        concat_axis=0,
        tiled=True,
    )

    grad_latent = (
        returned.reshape(sessions_here, bins_all, latent_width).astype(jnp.float32) * valid
    ).astype(jnp.bfloat16)
    slot_grads = jnp.einsum(
        "stk,std->skd", spikes, grad_latent, preferred_element_type=jnp.float32
    ).astype(jnp.bfloat16)
    slot_grads = slot_grads.reshape(slot_count, unit_block, latent_width)

    by_offset_grads = jnp.take(slot_grads, slot_of, axis=0, mode="clip")
    pieces = [by_offset_grads[0:1]]
    for offset in range(1, near):
        pieces.append(from_behind(by_offset_grads[offset : offset + 1], "dp", offset))
    middle = near // 2
    encoded_out, pieces[middle] = lax.optimization_barrier((encoded_out, pieces[middle]))
    contributions = jnp.concatenate(pieces, axis=0)
    onehot = (rows_in[:, None] == jnp.arange(table_rows, dtype=jnp.int32)[None, :]).astype(
        jnp.bfloat16
    )
    total = jnp.dot(
        onehot.T, contributions.reshape(near, -1), preferred_element_type=jnp.float32
    )
    total = total.astype(jnp.bfloat16).reshape(table_rows, unit_block, latent_width)
    return (encoded_out, total)


def solution(mesh):
    return jax.shard_map(
        on_device,
        mesh=mesh,
        in_specs=(
            P("dp", None, None),
            P("dp", None),
            P("dp"),
            P("dp", None, None),
            P(),
            P(),
            P(),
            P(None, "dp", None),
        ),
        out_specs=(P(None, "dp", None), P("dp", None, None)),
        check_vma=False,
    )
```

```python
import jax
import jax.numpy as jnp
from jax import lax
from jax.sharding import PartitionSpec as P


EPS = 1e-06


def from_behind(array, axis, by):
    count = lax.axis_size(axis)
    return lax.ppermute(array, axis, [(i, (i + by) % count) for i in range(count)])


def gelu_tanh(values):
    return jax.nn.gelu(values, approximate=True)


def encode_forward(latent_rows, norm_gain, w_in, w_out):
    inputs = latent_rows.astype(jnp.float32)
    mean_square = jnp.mean(inputs * inputs, axis=-1, keepdims=True)
    inverse_rms = lax.rsqrt(mean_square + EPS)
    normed = (inputs * inverse_rms * norm_gain).astype(jnp.bfloat16)
    hidden_pre = jnp.dot(normed, w_in, preferred_element_type=jnp.float32)
    activated = gelu_tanh(hidden_pre).astype(jnp.bfloat16)
    encoded = (inputs + jnp.dot(activated, w_out, preferred_element_type=jnp.float32)).astype(
        jnp.bfloat16
    )
    return encoded, (inputs, inverse_rms, hidden_pre)


def encode_backward(saved, norm_gain, w_in, w_out, cot_rows):
    inputs, inverse_rms, hidden_pre = saved
    grad_activated = lax.dot_general(
        cot_rows, w_out, (((1,), (1,)), ((), ())), preferred_element_type=jnp.float32
    )
    scale = jnp.sqrt(2.0 / jnp.pi).astype(jnp.float32)
    square = hidden_pre * hidden_pre
    tanh_inner = jnp.tanh(scale * (hidden_pre + 0.044715 * square * hidden_pre))
    slope = 0.5 * (1.0 + tanh_inner) + 0.5 * hidden_pre * (1.0 - tanh_inner * tanh_inner) * (
        scale * (1.0 + 3.0 * 0.044715 * square)
    )
    grad_hidden = lax.optimization_barrier((grad_activated * slope).astype(jnp.bfloat16))
    grad_normed = lax.dot_general(
        grad_hidden, w_in, (((1,), (1,)), ((), ())), preferred_element_type=jnp.float32
    )
    scaled = grad_normed * norm_gain
    grad_inputs = inverse_rms * scaled - inputs * (
        inverse_rms * inverse_rms * inverse_rms
    ) * jnp.mean(scaled * inputs, axis=-1, keepdims=True)
    returned = (cot_rows.astype(jnp.float32) + grad_inputs).astype(jnp.bfloat16)
    return returned


def on_device(spikes, block_lists, bin_counts, readin_table, norm_gain, w_in, w_out, cotangent):
    devices = lax.axis_size("dp")
    me = lax.axis_index("dp")
    sessions_here, bins_all, unit_columns = spikes.shape
    table_rows, unit_block, latent_width = readin_table.shape
    blocks_per = unit_columns // unit_block
    slot_count = sessions_here * blocks_per
    near = slot_count

    flat_lists = block_lists.reshape(slot_count)
    offsets = jnp.mod(flat_lists // table_rows - me, devices)
    slot_ids = jnp.arange(slot_count, dtype=jnp.int32)
    match = offsets[None, :] == jnp.arange(near, dtype=jnp.int32)[:, None]
    slot_of = jnp.sum(jnp.where(match, slot_ids[None, :], 0), axis=1)

    half = near // 2
    first_round = [flat_lists[None, :]] + [
        from_behind(flat_lists[None, :], "dp", shift) for shift in range(1, half)
    ]
    first_round = jnp.concatenate(first_round, axis=0)
    source_lists = jnp.concatenate([first_round, from_behind(first_round, "dp", half)], axis=0)
    source_lists = source_lists[:near]
    cotangent, source_lists = lax.optimization_barrier((cotangent, source_lists))
    mine = (source_lists // table_rows) == me
    rows_in = jnp.sum(jnp.where(mine, jnp.mod(source_lists, table_rows), 0), axis=1)

    to_send = jnp.take(readin_table, rows_in, axis=0, mode="clip")
    fetched = [to_send[0:1]]
    for offset in range(1, near):
        fetched.append(from_behind(to_send[offset : offset + 1], "dp", -offset))

    bins_here = cotangent.shape[1]
    cot_chunks = cotangent.reshape(devices, sessions_here, bins_here, latent_width)
    cot_chunks = lax.all_to_all(cot_chunks, "dp", split_axis=0, concat_axis=0, tiled=True)

    by_offset = jnp.concatenate(fetched, axis=0)
    by_slot = jnp.take(by_offset, offsets, axis=0, mode="clip")
    weights = by_slot.reshape(sessions_here, blocks_per * unit_block, latent_width)
    valid = (
        lax.broadcasted_iota(jnp.int32, (sessions_here, bins_all), 1) < bin_counts[:, None]
    ).astype(jnp.float32)[:, :, None]
    latent = jnp.einsum("stk,skd->std", spikes, weights, preferred_element_type=jnp.float32)
    latent = (latent * valid).astype(jnp.bfloat16)

    encoded, saved = encode_forward(latent.reshape(-1, latent_width), norm_gain, w_in, w_out)
    cot_chunks, encoded = lax.optimization_barrier((cot_chunks, encoded))
    cot_here = jnp.transpose(cot_chunks, (1, 0, 2, 3)).reshape(-1, latent_width)
    returned = encode_backward(saved, norm_gain, w_in, w_out, cot_here)
    encoded_out = lax.all_to_all(
        encoded.reshape(sessions_here, bins_all, latent_width),
        "dp",
        split_axis=1,
        concat_axis=0,
        tiled=True,
    )

    grad_latent = (
        returned.reshape(sessions_here, bins_all, latent_width).astype(jnp.float32) * valid
    ).astype(jnp.bfloat16)
    slot_grads = jnp.einsum(
        "stk,std->skd", spikes, grad_latent, preferred_element_type=jnp.float32
    ).astype(jnp.bfloat16)
    slot_grads = slot_grads.reshape(slot_count, unit_block, latent_width)

    by_offset_grads = jnp.take(slot_grads, slot_of, axis=0, mode="clip")
    pieces = [by_offset_grads[0:1]]
    for offset in range(1, near):
        pieces.append(from_behind(by_offset_grads[offset : offset + 1], "dp", offset))
    middle = near // 4
    encoded_out, pieces[middle] = lax.optimization_barrier((encoded_out, pieces[middle]))
    contributions = jnp.concatenate(pieces, axis=0)
    onehot = (rows_in[:, None] == jnp.arange(table_rows, dtype=jnp.int32)[None, :]).astype(
        jnp.bfloat16
    )
    total = jnp.dot(
        onehot.T, contributions.reshape(near, -1), preferred_element_type=jnp.float32
    )
    total = total.astype(jnp.bfloat16).reshape(table_rows, unit_block, latent_width)
    return (encoded_out, total)


def solution(mesh):
    return jax.shard_map(
        on_device,
        mesh=mesh,
        in_specs=(
            P("dp", None, None),
            P("dp", None),
            P("dp"),
            P("dp", None, None),
            P(),
            P(),
            P(),
            P(None, "dp", None),
        ),
        out_specs=(P(None, "dp", None), P("dp", None, None)),
        check_vma=False,
    )
```
